512 devices in a mesh: sec: 2 (over core), seq: 32 (over z, y_lo), rep: 8 (over x, y_hi).
Axes of the slice: x: 4, y: 4 (y_hi: 2, y_lo: 2; y = y_hi * 2 + y_lo), z: 16, core: 2. Of those that a mesh axis runs over, the one named last changes fastest.
Arguments:
- head_query: bfloat16 [64, 24, 1536, 128], P(('sec', 'rep'), None, 'seq'), may hold values from -4.5 to 4.5
- head_keys: bfloat16 [64, 24, 1536, 128], P(('sec', 'rep'), None, 'seq'), may hold values from -4.5 to 4.5
- head_values: bfloat16 [64, 24, 1536, 128], P(('sec', 'rep'), None, 'seq'), may hold values from -6 to 6
- mod_shift: float32 [64, 3072], P(('sec', 'rep')), may hold values from -3 to 3
- mod_scale: float32 [64, 3072], P(('sec', 'rep')), may hold values from -0.9 to 0.9
- final_weight: bfloat16 [3072, 64], replicated, may hold values from -0.109375 to 0.109375
- final_bias: float32 [64], replicated, may hold values from -3 to 3
- noisy_latent: float32 [64, 3, 64, 512], P(('sec', 'rep'), None, 'seq'), may hold values from -7.2 to 7.2
- step_index: int32 [64], P(('sec', 'rep')), may hold values from 46 to 49
- clip_order: int32 [64], replicated, may hold values from 0 to 63, each once
- conv_weight: bfloat16 [3, 3, 3, 16, 512], replicated, may hold values from -0.3125 to 0.3125
- conv_bias: float32 [512], replicated, may hold values from -3 to 3
- group_gain: float32 [512], replicated, may hold values from 0.1 to 1.9
- group_shift: float32 [512], replicated, may hold values from -3 to 3
Outputs:
- denoised: float32 [64, 3, 64, 512], P(('sec', 'rep'), None, 'seq')
- features: bfloat16 [64, 3, 64, 16384], P(('sec', 'rep'), None, 'seq')
The draws below stay inside these ranges and needn't reach their ends.
All inputs are finite; a program needn't handle non-finite values.
Results may differ from the reference program's by a relative error of at most 0.005.
Values may be sent and summed in bfloat16 or wider, within the bound.
No kernel may reach another device: no remote copies, remote signals or barrier semaphores. Data moves between devices by JAX's collectives and lax.ppermute only.
A program may use at most 128 MiB of HBM per device.

```python
import math
import jax
import jax.numpy as jnp
from jax import lax

HEADS = 24
HEAD_DIM = 128
LAT_CH = 16
VAE_CH = 512
GROUPS = 32
FRAMES = 3
PATCH_W = 16
NSTEPS = 50
DIM = 3072
PATCH_OUT = 64
SEQ_LEN = 1536
CLIPS_ALL = 64
LAT_H = 64
LAT_W = 32


def paired_fields(key):
    shape = (CLIPS_ALL, HEADS, SEQ_LEN, HEAD_DIM)
    query_field = jnp.clip(jax.random.normal(jax.random.fold_in(key, 21), shape), -4.5, 4.5)
    keys_field = jnp.clip(jax.random.normal(jax.random.fold_in(key, 22), shape), -4.5, 4.5)
    return (query_field, keys_field)


def draw_head_query(key, part):
    return paired_fields(key)[0].astype(jnp.bfloat16)


def draw_head_keys(key, part):
    return paired_fields(key)[1].astype(jnp.bfloat16)


def draw_noisy_latent(key, part):
    shape = (CLIPS_ALL, FRAMES, LAT_H, LAT_W * LAT_CH)
    height = jnp.arange(LAT_H, dtype=jnp.float32)[None, None, :, None] / max(LAT_H - 1, 1)
    values = jnp.clip(jax.random.normal(jax.random.fold_in(key, 33), shape), -4.0, 4.0) * (0.6 + 1.2 * height)
    return values


def place_ends(values, stream_key, least, largest):
    index_at = [jax.random.randint(jax.random.fold_in(stream_key, axis), (), 0, length) for axis, length in enumerate(values.shape)]
    longest = values.shape.index(max(values.shape))
    next_to = index_at[:longest] + [(index_at[longest] + 1) % values.shape[longest]] + index_at[longest + 1:]
    return values.at[tuple(index_at)].set(least).at[tuple(next_to)].set(largest)


def shard_levels(key, shape, pieces, smallest, top_value):
    gain, own = 1.0, jax.random.fold_in(key, 6)
    for dim, blocks in pieces:
        heights = jnp.exp(jax.random.uniform(jax.random.fold_in(own, dim), (blocks,), jnp.float32, smallest / len(pieces), top_value / len(pieces)))
        gain = gain * jnp.repeat(heights, shape[dim] // blocks).reshape([-1 if axis == dim else 1 for axis in range(len(shape))])
    return gain


def scatter_about(rng, extent, scale, reach, shards=(), kind=jnp.bfloat16):
    entries = jax.random.normal(rng, extent, jnp.float32) * scale
    if len(shards) > 0:
        entries = shard_levels(rng, extent, shards, -0.22, 0.18) * entries
    return jnp.clip(entries, min=-reach, max=reach).astype(kind)


def setup_inputs(seed: int = 0) -> dict:
    key_of = jax.random.split(jax.random.key(seed), 15)
    return {
        "head_query": draw_head_query(jax.random.fold_in(key_of[14], 71), 0),
        "head_keys": draw_head_keys(jax.random.fold_in(key_of[14], 71), 0),
        "head_values": scatter_about(key_of[2], (CLIPS_ALL, HEADS, SEQ_LEN, HEAD_DIM), 1.0, 6.0, ((0, 16), (2, 32))),
        "mod_shift": scatter_about(key_of[3], (CLIPS_ALL, DIM), 0.5, 3.0, ((0, 16),), jnp.float32),
        "mod_scale": scatter_about(key_of[4], (CLIPS_ALL, DIM), 0.3, 0.9, ((0, 16),), jnp.float32),
        "final_weight": scatter_about(key_of[5], (DIM, PATCH_OUT), DIM ** -0.5, 0.109375),
        "final_bias": scatter_about(key_of[6], (PATCH_OUT,), 1.0, 3.0, (), jnp.float32),
        "noisy_latent": draw_noisy_latent(jax.random.fold_in(key_of[14], 71), 0),
        "step_index": place_ends(jax.random.randint(key_of[8], (CLIPS_ALL,), NSTEPS - 4, NSTEPS), jax.random.fold_in(key_of[8], 1), NSTEPS - 4, NSTEPS - 1).astype(jnp.int32),
        "clip_order": jax.random.permutation(key_of[9], CLIPS_ALL).astype(jnp.int32),
        "conv_weight": scatter_about(key_of[10], (3, 3, 3, LAT_CH, VAE_CH), (27 * LAT_CH) ** -0.5, 0.3125),
        "conv_bias": scatter_about(key_of[11], (VAE_CH,), 0.5, 3.0, (), jnp.float32),
        "group_gain": jnp.clip(1.0 + 0.18 * jax.random.normal(key_of[12], (VAE_CH,), jnp.float32), 0.1, 1.9),
        "group_shift": scatter_about(key_of[13], (VAE_CH,), 0.5, 3.0, (), jnp.float32),
    }


eps_norm = 1e-06
shift_factor = 7.0

def attend_unit(operands):
    query_rows, key_rows, value_rows = operands
    length = query_rows.shape[0]
    block = math.gcd(length, 512)
    scale = 1.0 / math.sqrt(query_rows.shape[1])
    blocks = query_rows.reshape(length // block, block, query_rows.shape[1])

    def one_block(rows):
        scores = jnp.dot(rows, key_rows.T, preferred_element_type=jnp.float32) * scale
        top = lax.optimization_barrier(jnp.max(scores, axis=1, keepdims=True))
        expd = jnp.exp(scores - top)
        weights = (expd / lax.optimization_barrier(jnp.sum(expd, axis=1, keepdims=True))).astype(jnp.bfloat16)
        return jnp.dot(weights, value_rows, preferred_element_type=jnp.float32).astype(jnp.bfloat16)
    return lax.map(one_block, blocks).reshape(length, query_rows.shape[1])

def sigma_level(index):
    level = 1.0 - index.astype(jnp.float32) / NSTEPS
    return shift_factor * level / (1.0 + (shift_factor - 1.0) * level)

def causal_columns(rimmed):
    clips, frames, rows_rim, wide = rimmed.shape
    width = wide // LAT_CH
    grid = rimmed.reshape(clips, frames, rows_rim, width, LAT_CH)
    first = grid[:, :1]
    grid = jnp.concatenate([first, first, grid], axis=1)
    grid = jnp.pad(grid, ((0, 0), (0, 0), (0, 0), (1, 1), (0, 0)), mode='edge')
    taps = []
    for tap_time in range(3):
        for tap_row in range(3):
            for tap_col in range(3):
                taps.append(grid[:, tap_time:tap_time + frames, tap_row:tap_row + rows_rim - 2, tap_col:tap_col + width, :])
    return jnp.stack(taps, axis=4).reshape(clips, frames, rows_rim - 2, width, 27 * LAT_CH)

def reference(head_query, head_keys, head_values, mod_shift, mod_scale, final_weight, final_bias, noisy_latent, step_index, clip_order, conv_weight, conv_bias, group_gain, group_shift):
    clips_all = head_query.shape[0]
    seq_len = head_query.shape[2]
    units = clips_all * HEADS
    attention = lax.map(attend_unit, (head_query.reshape(units, seq_len, HEAD_DIM), head_keys.reshape(units, seq_len, HEAD_DIM), head_values.reshape(units, seq_len, HEAD_DIM)))
    attention = attention.reshape(clips_all, HEADS, seq_len, HEAD_DIM)
    weights3 = final_weight.astype(jnp.float32).reshape(HEADS, HEAD_DIM, PATCH_OUT)

    def final_layer(items):
        heads, scale_row, shift_row = items
        heads = heads.astype(jnp.float32)
        mean = lax.optimization_barrier(jnp.mean(heads, axis=(0, 2), keepdims=True))
        spread = lax.optimization_barrier(jnp.mean(jnp.square(heads - mean), axis=(0, 2), keepdims=True))
        normed = (heads - mean) * lax.rsqrt(spread + eps_norm)
        modulated = normed * (1.0 + scale_row.reshape(HEADS, 1, HEAD_DIM)) + shift_row.reshape(HEADS, 1, HEAD_DIM)
        return jnp.einsum('htd,hdo->to', modulated, weights3, precision=lax.Precision.HIGHEST) + final_bias
    velocity = lax.map(final_layer, (attention, mod_scale, mod_shift))
    lat_h = noisy_latent.shape[2]
    patch_rows = lat_h // 2
    velocity = velocity.reshape(clips_all, patch_rows, FRAMES, PATCH_W, 2, 2, LAT_CH)
    velocity = jnp.transpose(velocity, (0, 2, 1, 4, 3, 5, 6)).reshape(noisy_latent.shape)
    step = sigma_level(step_index + 1) - sigma_level(step_index)
    denoised = noisy_latent + step[:, None, None, None] * velocity
    decoder_in = denoised.astype(jnp.bfloat16)
    picked = jnp.take(decoder_in, clip_order, axis=0)
    rimmed = jnp.pad(picked, ((0, 0), (0, 0), (1, 1), (0, 0)), mode='edge')
    columns = causal_columns(rimmed)
    flat_weight = conv_weight.reshape(27 * LAT_CH, VAE_CH)
    conv_out = jnp.dot(columns.reshape(-1, 27 * LAT_CH), flat_weight, preferred_element_type=jnp.float32) + conv_bias
    conv_out = conv_out.reshape(clips_all, -1, GROUPS, VAE_CH // GROUPS)
    mean = lax.optimization_barrier(jnp.mean(conv_out, axis=(1, 3), keepdims=True))
    spread = lax.optimization_barrier(jnp.mean(jnp.square(conv_out - mean), axis=(1, 3), keepdims=True))
    normed = ((conv_out - mean) * lax.rsqrt(spread + eps_norm)).reshape(clips_all, -1, VAE_CH)
    features = jax.nn.silu(normed * group_gain + group_shift).astype(jnp.bfloat16)
    features = features.reshape(clips_all, FRAMES, lat_h, LAT_W * VAE_CH)
    return (denoised, features)
```

```python
import math

import jax
import jax.numpy as jnp
from jax import lax
from jax.sharding import PartitionSpec as P

HEADS = 24
HEAD_DIM = 128
LAT_CH = 16
VAE_CH = 512
GROUPS = 32
FRAMES = 3
PATCH_W = 16
NSTEPS = 50
PATCH_OUT = 64
LAT_W = 32


eps_norm = 1e-06
shift_factor = 7.0


def extended(cells, sides, width):
    for axis, dim in sides:
        count = lax.axis_size(axis)
        ends = count - 1
        head = lax.slice_in_dim(cells, 0, width, axis=dim)
        tail = lax.slice_in_dim(cells, cells.shape[dim] - width, cells.shape[dim], axis=dim)
        cells = jnp.concatenate(
            [
                lax.ppermute(tail, axis, [(i, (i + 1) % count) for i in range(ends)]),
                cells,
                lax.ppermute(head, axis, [((i + 1) % count, i) for i in range(ends)]),
            ],
            axis=dim,
        )
    return cells


def butterfly_gather(block, axis):
    count = lax.axis_size(axis)
    me = lax.axis_index(axis)
    held = block[None]
    step = 1
    while step < count:
        other = lax.ppermute(held, axis, [(i, i ^ step) for i in range(count)])
        low = (me // step) % 2 == 0
        held = jnp.where(
            low,
            jnp.concatenate([held, other], axis=0),
            jnp.concatenate([other, held], axis=0),
        )
        step *= 2
    return held.reshape((count * block.shape[0],) + block.shape[1:])


def butterfly_moments(mean, m2, count, axis):
    size = lax.axis_size(axis)
    step = 1
    while step < size:
        pair = lax.ppermute(jnp.stack([mean, m2]), axis, [(i, i ^ step) for i in range(size)])
        other_mean, other_m2 = pair[0], pair[1]
        gap = mean - other_mean
        m2 = (m2 + other_m2) + jnp.square(gap) * (0.5 * count * step)
        mean = (mean + other_mean) * 0.5
        step *= 2
    return mean, m2


def attend_unit(operands):
    query_rows, key_rows, value_rows = operands
    length = query_rows.shape[0]
    block = math.gcd(length, 512)
    scale = 1.0 / math.sqrt(query_rows.shape[1])
    blocks = query_rows.reshape(length // block, block, query_rows.shape[1])

    def one_block(rows):
        scores = jnp.dot(rows, key_rows.T, preferred_element_type=jnp.float32) * scale
        top = jnp.max(scores, axis=1, keepdims=True)
        expd = jnp.exp(scores - top)
        weights = (expd / jnp.sum(expd, axis=1, keepdims=True)).astype(jnp.bfloat16)
        return jnp.dot(weights, value_rows, preferred_element_type=jnp.float32).astype(jnp.bfloat16)

    return lax.map(one_block, blocks).reshape(length, query_rows.shape[1])


def sigma_level(index):
    level = 1.0 - index.astype(jnp.float32) / NSTEPS
    return shift_factor * level / (1.0 + (shift_factor - 1.0) * level)


def causal_columns(rimmed):
    clips, frames, rows_rim, wide = rimmed.shape
    width = wide // LAT_CH
    grid = rimmed.reshape(clips, frames, rows_rim, width, LAT_CH)
    first = grid[:, :1]
    grid = jnp.concatenate([first, first, grid], axis=1)
    grid = jnp.pad(grid, ((0, 0), (0, 0), (0, 0), (1, 1), (0, 0)), mode="edge")
    taps = []
    for tap_time in range(3):
        for tap_row in range(3):
            for tap_col in range(3):
                taps.append(
                    grid[
                        :,
                        tap_time : tap_time + frames,
                        tap_row : tap_row + rows_rim - 2,
                        tap_col : tap_col + width,
                        :,
                    ]
                )
    return jnp.stack(taps, axis=4).reshape(clips, frames, rows_rim - 2, width, 27 * LAT_CH)


def edge_rows(rimmed):
    position = lax.axis_index("seq")
    last_index = lax.axis_size("seq") - 1
    upper = jnp.where(position == 0, rimmed[:, :, 1:2], rimmed[:, :, 0:1])
    lower = jnp.where(position == last_index, rimmed[:, :, -2:-1], rimmed[:, :, -1:])
    return jnp.concatenate([upper, rimmed[:, :, 1:-1], lower], axis=2)


def shards(
    head_query,
    head_keys,
    head_values,
    mod_shift,
    mod_scale,
    final_weight,
    final_bias,
    noisy_latent,
    step_index,
    clip_order,
    conv_weight,
    conv_bias,
    group_gain,
    group_shift,
):
    n_seq = lax.axis_size("seq")
    clips = head_query.shape[0]
    tok_dev = head_query.shape[2]
    units_local = clips * HEADS // n_seq
    stacked = jnp.stack(
        [
            head_query.reshape(n_seq, units_local, tok_dev, HEAD_DIM),
            head_keys.reshape(n_seq, units_local, tok_dev, HEAD_DIM),
            head_values.reshape(n_seq, units_local, tok_dev, HEAD_DIM),
        ],
        axis=1,
    )
    parts = lax.all_to_all(stacked, "seq", split_axis=0, concat_axis=3, tiled=True)
    outputs = lax.map(attend_unit, (parts[0, 0], parts[0, 1], parts[0, 2]))[None]
    mixed = lax.all_to_all(outputs, "seq", split_axis=2, concat_axis=0, tiled=True)
    heads = mixed.reshape(clips, HEADS, tok_dev, HEAD_DIM).astype(jnp.float32)
    tokens = jnp.transpose(heads, (0, 2, 1, 3)).reshape(clips, tok_dev, HEADS * HEAD_DIM)
    mean = jnp.mean(tokens, axis=2, keepdims=True)
    spread = jnp.mean(jnp.square(tokens - mean), axis=2, keepdims=True)
    normed = (tokens - mean) * lax.rsqrt(spread + eps_norm)
    modulated = normed * (1.0 + mod_scale[:, None, :]) + mod_shift[:, None, :]
    velocity = (
        jnp.einsum(
            "ctk,ko->cto",
            modulated,
            final_weight.astype(jnp.float32),
            precision=lax.Precision.HIGHEST,
        )
        + final_bias
    )
    rows_dev = noisy_latent.shape[2]
    velocity = velocity.reshape(clips, rows_dev // 2, FRAMES, PATCH_W, 2, 2, LAT_CH)
    velocity = jnp.transpose(velocity, (0, 2, 1, 4, 3, 5, 6)).reshape(noisy_latent.shape)
    step = sigma_level(step_index + 1) - sigma_level(step_index)
    denoised = noisy_latent + step[:, None, None, None] * velocity
    decoder_in = denoised.astype(jnp.bfloat16)
    group_index = lax.axis_index(("sec", "rep"))
    wanted = lax.dynamic_slice_in_dim(clip_order, group_index * clips, clips)
    everyone = butterfly_gather(decoder_in, ("sec", "rep"))
    picked = jnp.take(everyone, wanted, axis=0)
    rimmed = edge_rows(extended(picked, (("seq", 2),), 1))
    columns = causal_columns(rimmed)
    flat_weight = conv_weight.reshape(27 * LAT_CH, VAE_CH)
    conv_out = (
        jnp.dot(columns.reshape(-1, 27 * LAT_CH), flat_weight, preferred_element_type=jnp.float32)
        + conv_bias
    )
    conv_out = conv_out.reshape(clips, -1, GROUPS, VAE_CH // GROUPS)
    count = conv_out.shape[1] * (VAE_CH // GROUPS)
    local_mean = jnp.sum(conv_out, axis=(1, 3)) / count
    centered_local = conv_out - local_mean[:, None, :, None]
    local_m2 = jnp.sum(jnp.square(centered_local), axis=(1, 3))
    mean, m2 = butterfly_moments(local_mean, local_m2, count, "seq")
    centered = conv_out - mean[:, None, :, None]
    spread = m2 / (count * n_seq)
    normed = (centered * lax.rsqrt(spread + eps_norm)[:, None, :, None]).reshape(clips, -1, VAE_CH)
    features = jax.nn.silu(normed * group_gain + group_shift).astype(jnp.bfloat16)
    features = features.reshape(clips, FRAMES, rows_dev, LAT_W * VAE_CH)
    return (denoised, features)


def solution(mesh):
    placed = (
        P(("sec", "rep"), None, "seq", None),
        P(("sec", "rep"), None, "seq", None),
        P(("sec", "rep"), None, "seq", None),
        P(("sec", "rep"), None),
        P(("sec", "rep"), None),
        P(),
        P(),
        P(("sec", "rep"), None, "seq", None),
        P(("sec", "rep")),
        P(),
        P(),
        P(),
        P(),
        P(),
    )
    return jax.shard_map(
        shards,
        mesh=mesh,
        in_specs=placed,
        out_specs=(P(("sec", "rep"), None, "seq", None), P(("sec", "rep"), None, "seq", None)),
        check_vma=False,
    )
```

```python
import math

import jax
import jax.numpy as jnp
from jax import lax
from jax.sharding import PartitionSpec as P

HEADS = 24
HEAD_DIM = 128
LAT_CH = 16
VAE_CH = 512
GROUPS = 32
FRAMES = 3
PATCH_W = 16
NSTEPS = 50
PATCH_OUT = 64
LAT_W = 32


eps_norm = 1e-06
shift_factor = 7.0


def extended(cells, sides, width):
    for axis, dim in sides:
        count = lax.axis_size(axis)
        ends = count - 1
        head = lax.slice_in_dim(cells, 0, width, axis=dim)
        tail = lax.slice_in_dim(cells, cells.shape[dim] - width, cells.shape[dim], axis=dim)
        cells = jnp.concatenate(
            [
                lax.ppermute(tail, axis, [(i, (i + 1) % count) for i in range(ends)]),
                cells,
                lax.ppermute(head, axis, [((i + 1) % count, i) for i in range(ends)]),
            ],
            axis=dim,
        )
    return cells


def butterfly_gather(block, axis):
    count = lax.axis_size(axis)
    me = lax.axis_index(axis)
    held = block[None]
    step = 1
    while step < count:
        other = lax.ppermute(held, axis, [(i, i ^ step) for i in range(count)])
        low = (me // step) % 2 == 0
        held = jnp.where(
            low,
            jnp.concatenate([held, other], axis=0),
            jnp.concatenate([other, held], axis=0),
        )
        step *= 2
    return held.reshape((count * block.shape[0],) + block.shape[1:])


def butterfly_moments(mean, m2, count, axis):
    size = lax.axis_size(axis)
    step = 1
    while step < size:
        pair = lax.ppermute(jnp.stack([mean, m2]), axis, [(i, i ^ step) for i in range(size)])
        other_mean, other_m2 = pair[0], pair[1]
        gap = mean - other_mean
        m2 = (m2 + other_m2) + jnp.square(gap) * (0.5 * count * step)
        mean = (mean + other_mean) * 0.5
        step *= 2
    return mean, m2


def attend_unit(operands):
    query_rows, key_rows, value_rows = operands
    length = query_rows.shape[0]
    block = math.gcd(length, 512)
    scale = 1.0 / math.sqrt(query_rows.shape[1])
    blocks = query_rows.reshape(length // block, block, query_rows.shape[1])

    def one_block(rows):
        scores = jnp.dot(rows, key_rows.T, preferred_element_type=jnp.float32) * scale
        top = jnp.max(scores, axis=1, keepdims=True)
        expd = jnp.exp(scores - top)
        weights = (expd / jnp.sum(expd, axis=1, keepdims=True)).astype(jnp.bfloat16)
        return jnp.dot(weights, value_rows, preferred_element_type=jnp.float32).astype(jnp.bfloat16)

    return lax.map(one_block, blocks).reshape(length, query_rows.shape[1])


def sigma_level(index):
    level = 1.0 - index.astype(jnp.float32) / NSTEPS
    return shift_factor * level / (1.0 + (shift_factor - 1.0) * level)


def causal_columns(rimmed):
    clips, frames, rows_rim, wide = rimmed.shape
    width = wide // LAT_CH
    grid = rimmed.reshape(clips, frames, rows_rim, width, LAT_CH)
    first = grid[:, :1]
    grid = jnp.concatenate([first, first, grid], axis=1)
    grid = jnp.pad(grid, ((0, 0), (0, 0), (0, 0), (1, 1), (0, 0)), mode="edge")
    taps = []
    for tap_time in range(3):
        for tap_row in range(3):
            for tap_col in range(3):
                taps.append(
                    grid[
                        :,
                        tap_time : tap_time + frames,
                        tap_row : tap_row + rows_rim - 2,
                        tap_col : tap_col + width,
                        :,
                    ]
                )
    return jnp.stack(taps, axis=4).reshape(clips, frames, rows_rim - 2, width, 27 * LAT_CH)


def edge_rows(rimmed):
    position = lax.axis_index("seq")
    last_index = lax.axis_size("seq") - 1
    upper = jnp.where(position == 0, rimmed[:, :, 1:2], rimmed[:, :, 0:1])
    lower = jnp.where(position == last_index, rimmed[:, :, -2:-1], rimmed[:, :, -1:])
    return jnp.concatenate([upper, rimmed[:, :, 1:-1], lower], axis=2)


def shards(
    head_query,
    head_keys,
    head_values,
    mod_shift,
    mod_scale,
    final_weight,
    final_bias,
    noisy_latent,
    step_index,
    clip_order,
    conv_weight,
    conv_bias,
    group_gain,
    group_shift,
):
    n_seq = lax.axis_size("seq")
    clips = head_query.shape[0]
    tok_dev = head_query.shape[2]
    units_local = clips * HEADS // n_seq
    stacked = jnp.stack(
        [
            head_query.reshape(n_seq, units_local, tok_dev, HEAD_DIM),
            head_keys.reshape(n_seq, units_local, tok_dev, HEAD_DIM),
            head_values.reshape(n_seq, units_local, tok_dev, HEAD_DIM),
        ],
        axis=1,
    )
    parts = lax.all_to_all(stacked, "seq", split_axis=0, concat_axis=3, tiled=True)
    outputs = lax.map(attend_unit, (parts[0, 0], parts[0, 1], parts[0, 2]))
    seq_len = outputs.shape[1]
    chunks = HEADS // units_local
    width = units_local * HEAD_DIM
    me = lax.axis_index("seq")
    own_clip = me // chunks
    own_chunk = me % chunks
    weight = final_weight.astype(jnp.float32)
    x = jnp.transpose(outputs.astype(jnp.float32), (1, 0, 2)).reshape(seq_len, width)
    part_mean = jnp.mean(x, axis=1, keepdims=True)
    part_dev = x - part_mean
    part_m2 = jnp.sum(jnp.square(part_dev), axis=1, keepdims=True)
    scale_row = lax.dynamic_slice_in_dim(mod_scale, own_clip, 1, axis=0)[0]
    scale_part = lax.dynamic_slice_in_dim(scale_row, own_chunk * width, width)
    weight_part = lax.dynamic_slice_in_dim(weight, own_chunk * width, width, axis=0)
    folded = (1.0 + scale_part)[:, None] * weight_part
    partial = jnp.dot(part_dev, folded, precision=lax.Precision.HIGHEST)
    packed = jnp.concatenate([partial, part_mean, part_m2], axis=1)
    fields = packed.shape[1]
    packed = packed.reshape(n_seq, tok_dev * fields)
    recv = lax.all_to_all(packed, "seq", split_axis=0, concat_axis=0, tiled=True)
    recv = recv.reshape(clips, chunks, tok_dev, fields)
    partials = recv[..., :PATCH_OUT]
    means = recv[..., PATCH_OUT]
    m2s = recv[..., PATCH_OUT + 1]
    mean = jnp.mean(means, axis=1)
    gaps = means - mean[:, None, :]
    m2 = jnp.sum(m2s, axis=1) + width * jnp.sum(jnp.square(gaps), axis=1)
    rstd = lax.rsqrt(m2 / (HEADS * HEAD_DIM) + eps_norm)
    folded_all = jnp.einsum(
        "cjk,jko->cjo",
        (1.0 + mod_scale).reshape(clips, chunks, width),
        weight.reshape(chunks, width, PATCH_OUT),
        precision=lax.Precision.HIGHEST,
    )
    core = jnp.sum(partials, axis=1) + jnp.einsum(
        "cjt,cjo->cto", gaps, folded_all, precision=lax.Precision.HIGHEST
    )
    shift_proj = jnp.dot(mod_shift, weight, precision=lax.Precision.HIGHEST)
    velocity = rstd[..., None] * core + shift_proj[:, None, :] + final_bias
    rows_dev = noisy_latent.shape[2]
    velocity = velocity.reshape(clips, rows_dev // 2, FRAMES, PATCH_W, 2, 2, LAT_CH)
    velocity = jnp.transpose(velocity, (0, 2, 1, 4, 3, 5, 6)).reshape(noisy_latent.shape)
    step = sigma_level(step_index + 1) - sigma_level(step_index)
    denoised = noisy_latent + step[:, None, None, None] * velocity
    decoder_in = denoised.astype(jnp.bfloat16)
    group_index = lax.axis_index(("sec", "rep"))
    wanted = lax.dynamic_slice_in_dim(clip_order, group_index * clips, clips)
    everyone = butterfly_gather(decoder_in, ("sec", "rep"))
    picked = jnp.take(everyone, wanted, axis=0)
    rimmed = edge_rows(extended(picked, (("seq", 2),), 1))
    columns = causal_columns(rimmed)
    flat_weight = conv_weight.reshape(27 * LAT_CH, VAE_CH)
    conv_out = (
        jnp.dot(columns.reshape(-1, 27 * LAT_CH), flat_weight, preferred_element_type=jnp.float32)
        + conv_bias
    )
    conv_out = conv_out.reshape(clips, -1, GROUPS, VAE_CH // GROUPS)
    count = conv_out.shape[1] * (VAE_CH // GROUPS)
    local_mean = jnp.sum(conv_out, axis=(1, 3)) / count
    centered_local = conv_out - local_mean[:, None, :, None]
    local_m2 = jnp.sum(jnp.square(centered_local), axis=(1, 3))
    mean, m2 = butterfly_moments(local_mean, local_m2, count, "seq")
    centered = conv_out - mean[:, None, :, None]
    spread = m2 / (count * n_seq)
    normed = (centered * lax.rsqrt(spread + eps_norm)[:, None, :, None]).reshape(clips, -1, VAE_CH)
    features = jax.nn.silu(normed * group_gain + group_shift).astype(jnp.bfloat16)
    features = features.reshape(clips, FRAMES, rows_dev, LAT_W * VAE_CH)
    return (denoised, features)


def solution(mesh):
    placed = (
        P(("sec", "rep"), None, "seq", None),
        P(("sec", "rep"), None, "seq", None),
        P(("sec", "rep"), None, "seq", None),
        P(("sec", "rep"), None),
        P(("sec", "rep"), None),
        P(),
        P(),
        P(("sec", "rep"), None, "seq", None),
        P(("sec", "rep")),
        P(),
        P(),
        P(),
        P(),
        P(),
    )
    return jax.shard_map(
        shards,
        mesh=mesh,
        in_specs=placed,
        out_specs=(P(("sec", "rep"), None, "seq", None), P(("sec", "rep"), None, "seq", None)),
        check_vma=False,
    )
```

```python
import math

import jax
import jax.numpy as jnp
from jax import lax
from jax.sharding import PartitionSpec as P

HEADS = 24
HEAD_DIM = 128
LAT_CH = 16
VAE_CH = 512
GROUPS = 32
FRAMES = 3
PATCH_W = 16
NSTEPS = 50
PATCH_OUT = 64
LAT_W = 32


eps_norm = 1e-06
shift_factor = 7.0


def extended(cells, sides, width):
    for axis, dim in sides:
        count = lax.axis_size(axis)
        ends = count - 1
        head = lax.slice_in_dim(cells, 0, width, axis=dim)
        tail = lax.slice_in_dim(cells, cells.shape[dim] - width, cells.shape[dim], axis=dim)
        cells = jnp.concatenate(
            [
                lax.ppermute(tail, axis, [(i, (i + 1) % count) for i in range(ends)]),
                cells,
                lax.ppermute(head, axis, [((i + 1) % count, i) for i in range(ends)]),
            ],
            axis=dim,
        )
    return cells


def gather_all(block, axis):
    count = lax.axis_size(axis)
    copies = jnp.broadcast_to(block[None], (count,) + block.shape)
    return lax.all_to_all(copies, axis, 0, 0, tiled=True)


def butterfly_gather(block, axis):
    count = lax.axis_size(axis)
    me = lax.axis_index(axis)
    held = block[None]
    step = 1
    while step < count:
        other = lax.ppermute(held, axis, [(i, i ^ step) for i in range(count)])
        low = (me // step) % 2 == 0
        held = jnp.where(
            low,
            jnp.concatenate([held, other], axis=0),
            jnp.concatenate([other, held], axis=0),
        )
        step *= 2
    return held.reshape((count * block.shape[0],) + block.shape[1:])


def butterfly_moments(mean, m2, count, axis):
    size = lax.axis_size(axis)
    step = 1
    while step < size:
        pair = lax.ppermute(jnp.stack([mean, m2]), axis, [(i, i ^ step) for i in range(size)])
        other_mean, other_m2 = pair[0], pair[1]
        gap = mean - other_mean
        m2 = (m2 + other_m2) + jnp.square(gap) * (0.5 * count * step)
        mean = (mean + other_mean) * 0.5
        step *= 2
    return mean, m2


def attend_unit(operands):
    query_rows, key_rows, value_rows = operands
    length = query_rows.shape[0]
    block = math.gcd(length, 512)
    scale = 1.0 / math.sqrt(query_rows.shape[1])
    blocks = query_rows.reshape(length // block, block, query_rows.shape[1])

    def one_block(rows):
        scores = jnp.dot(rows, key_rows.T, preferred_element_type=jnp.float32) * scale
        top = jnp.max(scores, axis=1, keepdims=True)
        expd = jnp.exp(scores - top)
        weights = (expd / jnp.sum(expd, axis=1, keepdims=True)).astype(jnp.bfloat16)
        return jnp.dot(weights, value_rows, preferred_element_type=jnp.float32).astype(jnp.bfloat16)

    return lax.map(one_block, blocks).reshape(length, query_rows.shape[1])


def sigma_level(index):
    level = 1.0 - index.astype(jnp.float32) / NSTEPS
    return shift_factor * level / (1.0 + (shift_factor - 1.0) * level)


def causal_columns(rimmed):
    clips, frames, rows_rim, wide = rimmed.shape
    width = wide // LAT_CH
    grid = rimmed.reshape(clips, frames, rows_rim, width, LAT_CH)
    first = grid[:, :1]
    grid = jnp.concatenate([first, first, grid], axis=1)
    grid = jnp.pad(grid, ((0, 0), (0, 0), (0, 0), (1, 1), (0, 0)), mode="edge")
    taps = []
    for tap_time in range(3):
        for tap_row in range(3):
            for tap_col in range(3):
                taps.append(
                    grid[
                        :,
                        tap_time : tap_time + frames,
                        tap_row : tap_row + rows_rim - 2,
                        tap_col : tap_col + width,
                        :,
                    ]
                )
    return jnp.stack(taps, axis=4).reshape(clips, frames, rows_rim - 2, width, 27 * LAT_CH)


def edge_rows(rimmed):
    position = lax.axis_index("seq")
    last_index = lax.axis_size("seq") - 1
    upper = jnp.where(position == 0, rimmed[:, :, 1:2], rimmed[:, :, 0:1])
    lower = jnp.where(position == last_index, rimmed[:, :, -2:-1], rimmed[:, :, -1:])
    return jnp.concatenate([upper, rimmed[:, :, 1:-1], lower], axis=2)


def shards(
    head_query,
    head_keys,
    head_values,
    mod_shift,
    mod_scale,
    final_weight,
    final_bias,
    noisy_latent,
    step_index,
    clip_order,
    conv_weight,
    conv_bias,
    group_gain,
    group_shift,
):
    n_seq = lax.axis_size("seq")
    clips = head_query.shape[0]
    tok_dev = head_query.shape[2]
    units_local = clips * HEADS // n_seq
    stacked = jnp.stack(
        [
            head_query.reshape(n_seq, units_local, tok_dev, HEAD_DIM),
            head_keys.reshape(n_seq, units_local, tok_dev, HEAD_DIM),
            head_values.reshape(n_seq, units_local, tok_dev, HEAD_DIM),
        ],
        axis=1,
    )
    parts = lax.all_to_all(stacked, "seq", split_axis=0, concat_axis=3, tiled=True)
    outputs = lax.map(attend_unit, (parts[0, 0], parts[0, 1], parts[0, 2]))
    seq_len = outputs.shape[1]
    chunks = HEADS // units_local
    width = units_local * HEAD_DIM
    me = lax.axis_index("seq")
    own_clip = me // chunks
    own_chunk = me % chunks
    weight = final_weight.astype(jnp.float32)
    x = jnp.transpose(outputs.astype(jnp.float32), (1, 0, 2)).reshape(seq_len, width)
    part_mean = jnp.mean(x, axis=1, keepdims=True)
    part_dev = x - part_mean
    part_m2 = jnp.sum(jnp.square(part_dev), axis=1, keepdims=True)
    scale_row = lax.dynamic_slice_in_dim(mod_scale, own_clip, 1, axis=0)[0]
    scale_part = lax.dynamic_slice_in_dim(scale_row, own_chunk * width, width)
    weight_part = lax.dynamic_slice_in_dim(weight, own_chunk * width, width, axis=0)
    folded = (1.0 + scale_part)[:, None] * weight_part
    partial = jnp.dot(part_dev, folded, precision=lax.Precision.HIGHEST)
    packed = jnp.concatenate([partial, part_mean, part_m2], axis=1)
    fields = packed.shape[1]
    packed = packed.reshape(n_seq, tok_dev * fields)
    recv = lax.all_to_all(packed, "seq", split_axis=0, concat_axis=0, tiled=True)
    recv = recv.reshape(clips, chunks, tok_dev, fields)
    partials = recv[..., :PATCH_OUT]
    means = recv[..., PATCH_OUT]
    m2s = recv[..., PATCH_OUT + 1]
    mean = jnp.mean(means, axis=1)
    gaps = means - mean[:, None, :]
    m2 = jnp.sum(m2s, axis=1) + width * jnp.sum(jnp.square(gaps), axis=1)
    rstd = lax.rsqrt(m2 / (HEADS * HEAD_DIM) + eps_norm)
    folded_all = jnp.einsum(
        "cjk,jko->cjo",
        (1.0 + mod_scale).reshape(clips, chunks, width),
        weight.reshape(chunks, width, PATCH_OUT),
        precision=lax.Precision.HIGHEST,
    )
    core = jnp.sum(partials, axis=1) + jnp.einsum(
        "cjt,cjo->cto", gaps, folded_all, precision=lax.Precision.HIGHEST
    )
    shift_proj = jnp.dot(mod_shift, weight, precision=lax.Precision.HIGHEST)
    velocity = rstd[..., None] * core + shift_proj[:, None, :] + final_bias
    rows_dev = noisy_latent.shape[2]
    velocity = velocity.reshape(clips, rows_dev // 2, FRAMES, PATCH_W, 2, 2, LAT_CH)
    velocity = jnp.transpose(velocity, (0, 2, 1, 4, 3, 5, 6)).reshape(noisy_latent.shape)
    step = sigma_level(step_index + 1) - sigma_level(step_index)
    denoised = noisy_latent + step[:, None, None, None] * velocity
    decoder_in = denoised.astype(jnp.bfloat16)
    group_index = lax.axis_index(("sec", "rep"))
    wanted = lax.dynamic_slice_in_dim(clip_order, group_index * clips, clips)
    everyone = gather_all(decoder_in, ("sec", "rep"))
    everyone = everyone.reshape((-1,) + decoder_in.shape[1:])
    picked = jnp.take(everyone, wanted, axis=0)
    rimmed = edge_rows(extended(picked, (("seq", 2),), 1))
    grid = rimmed.reshape(clips, FRAMES, rimmed.shape[2], LAT_W, LAT_CH)
    first = grid[:, :1]
    grid = jnp.concatenate([first, first, grid], axis=1)
    grid = jnp.pad(grid, ((0, 0), (0, 0), (0, 0), (1, 1), (0, 0)), mode="edge")
    conv_out = lax.conv_general_dilated(
        grid,
        conv_weight,
        (1, 1, 1),
        "VALID",
        dimension_numbers=("NDHWC", "DHWIO", "NDHWC"),
        preferred_element_type=jnp.float32,
    )
    conv_out = conv_out.reshape(clips, -1, VAE_CH) + conv_bias
    conv_out = conv_out.reshape(clips, -1, GROUPS, VAE_CH // GROUPS)
    count = conv_out.shape[1] * (VAE_CH // GROUPS)
    local_mean = jnp.sum(conv_out, axis=(1, 3)) / count
    centered_local = conv_out - local_mean[:, None, :, None]
    local_m2 = jnp.sum(jnp.square(centered_local), axis=(1, 3))
    moments = gather_all(jnp.stack([local_mean, local_m2]), "seq")
    means, m2s = moments[:, 0], moments[:, 1]
    mean = jnp.mean(means, axis=0)
    m2 = jnp.sum(m2s, axis=0) + count * jnp.sum(jnp.square(means - mean), axis=0)
    centered = conv_out - mean[:, None, :, None]
    spread = m2 / (count * n_seq)
    normed = (centered * lax.rsqrt(spread + eps_norm)[:, None, :, None]).reshape(clips, -1, VAE_CH)
    features = jax.nn.silu(normed * group_gain + group_shift).astype(jnp.bfloat16)
    features = features.reshape(clips, FRAMES, rows_dev, LAT_W * VAE_CH)
    return (denoised, features)


def solution(mesh):
    placed = (
        P(("sec", "rep"), None, "seq", None),
        P(("sec", "rep"), None, "seq", None),
        P(("sec", "rep"), None, "seq", None),
        P(("sec", "rep"), None),
        P(("sec", "rep"), None),
        P(),
        P(),
        P(("sec", "rep"), None, "seq", None),
        P(("sec", "rep")),
        P(),
        P(),
        P(),
        P(),
        P(),
    )
    return jax.shard_map(
        shards,
        mesh=mesh,
        in_specs=placed,
        out_specs=(P(("sec", "rep"), None, "seq", None), P(("sec", "rep"), None, "seq", None)),
        check_vma=False,
    )
```

```python
import math

import jax
import jax.numpy as jnp
from jax import lax
from jax.sharding import PartitionSpec as P

HEADS = 24
HEAD_DIM = 128
LAT_CH = 16
VAE_CH = 512
GROUPS = 32
FRAMES = 3
PATCH_W = 16
NSTEPS = 50
PATCH_OUT = 64
LAT_W = 32


eps_norm = 1e-06
shift_factor = 7.0


def extended(cells, sides, width):
    for axis, dim in sides:
        count = lax.axis_size(axis)
        ends = count - 1
        head = lax.slice_in_dim(cells, 0, width, axis=dim)
        tail = lax.slice_in_dim(cells, cells.shape[dim] - width, cells.shape[dim], axis=dim)
        cells = jnp.concatenate(
            [
                lax.ppermute(tail, axis, [(i, (i + 1) % count) for i in range(ends)]),
                cells,
                lax.ppermute(head, axis, [((i + 1) % count, i) for i in range(ends)]),
            ],
            axis=dim,
        )
    return cells


def gather_all(block, axis):
    count = lax.axis_size(axis)
    copies = jnp.broadcast_to(block[None], (count,) + block.shape)
    return lax.all_to_all(copies, axis, 0, 0, tiled=True)


def butterfly_gather(block, axis):
    count = lax.axis_size(axis)
    me = lax.axis_index(axis)
    held = block[None]
    step = 1
    while step < count:
        other = lax.ppermute(held, axis, [(i, i ^ step) for i in range(count)])
        low = (me // step) % 2 == 0
        held = jnp.where(
            low,
            jnp.concatenate([held, other], axis=0),
            jnp.concatenate([other, held], axis=0),
        )
        step *= 2
    return held.reshape((count * block.shape[0],) + block.shape[1:])


def butterfly_moments(mean, m2, count, axis):
    size = lax.axis_size(axis)
    step = 1
    while step < size:
        pair = lax.ppermute(jnp.stack([mean, m2]), axis, [(i, i ^ step) for i in range(size)])
        other_mean, other_m2 = pair[0], pair[1]
        gap = mean - other_mean
        m2 = (m2 + other_m2) + jnp.square(gap) * (0.5 * count * step)
        mean = (mean + other_mean) * 0.5
        step *= 2
    return mean, m2


def attend_unit(operands):
    query_rows, key_rows, value_rows = operands
    length = query_rows.shape[0]
    block = math.gcd(length, 512)
    scale = 1.0 / math.sqrt(query_rows.shape[1])
    blocks = query_rows.reshape(length // block, block, query_rows.shape[1])

    def one_block(rows):
        scores = jnp.dot(rows, key_rows.T, preferred_element_type=jnp.float32) * scale
        top = jnp.max(scores, axis=1, keepdims=True)
        expd = jnp.exp(scores - top)
        weights = (expd / jnp.sum(expd, axis=1, keepdims=True)).astype(jnp.bfloat16)
        return jnp.dot(weights, value_rows, preferred_element_type=jnp.float32).astype(jnp.bfloat16)

    return lax.map(one_block, blocks).reshape(length, query_rows.shape[1])


def sigma_level(index):
    level = 1.0 - index.astype(jnp.float32) / NSTEPS
    return shift_factor * level / (1.0 + (shift_factor - 1.0) * level)


def causal_columns(rimmed):
    clips, frames, rows_rim, wide = rimmed.shape
    width = wide // LAT_CH
    grid = rimmed.reshape(clips, frames, rows_rim, width, LAT_CH)
    first = grid[:, :1]
    grid = jnp.concatenate([first, first, grid], axis=1)
    grid = jnp.pad(grid, ((0, 0), (0, 0), (0, 0), (1, 1), (0, 0)), mode="edge")
    taps = []
    for tap_time in range(3):
        for tap_row in range(3):
            for tap_col in range(3):
                taps.append(
                    grid[
                        :,
                        tap_time : tap_time + frames,
                        tap_row : tap_row + rows_rim - 2,
                        tap_col : tap_col + width,
                        :,
                    ]
                )
    return jnp.stack(taps, axis=4).reshape(clips, frames, rows_rim - 2, width, 27 * LAT_CH)


def edge_rows(rimmed):
    position = lax.axis_index("seq")
    last_index = lax.axis_size("seq") - 1
    upper = jnp.where(position == 0, rimmed[:, :, 1:2], rimmed[:, :, 0:1])
    lower = jnp.where(position == last_index, rimmed[:, :, -2:-1], rimmed[:, :, -1:])
    return jnp.concatenate([upper, rimmed[:, :, 1:-1], lower], axis=2)


def shards(
    head_query,
    head_keys,
    head_values,
    mod_shift,
    mod_scale,
    final_weight,
    final_bias,
    noisy_latent,
    step_index,
    clip_order,
    conv_weight,
    conv_bias,
    group_gain,
    group_shift,
):
    n_seq = lax.axis_size("seq")
    clips = head_query.shape[0]
    tok_dev = head_query.shape[2]
    units_local = clips * HEADS // n_seq
    query_four = head_query.reshape(n_seq, units_local, tok_dev, HEAD_DIM)
    keys_four = head_keys.reshape(n_seq, units_local, tok_dev, HEAD_DIM)
    values_four = head_values.reshape(n_seq, units_local, tok_dev, HEAD_DIM)
    attended = []
    for unit in range(units_local):
        stacked = jnp.stack(
            [query_four[:, unit], keys_four[:, unit], values_four[:, unit]], axis=1
        )
        part = lax.all_to_all(stacked, "seq", split_axis=0, concat_axis=2, tiled=True)
        attended.append(attend_unit((part[0, 0], part[0, 1], part[0, 2])))
    outputs = jnp.stack(attended)
    seq_len = outputs.shape[1]
    chunks = HEADS // units_local
    width = units_local * HEAD_DIM
    me = lax.axis_index("seq")
    own_clip = me // chunks
    own_chunk = me % chunks
    weight = final_weight.astype(jnp.float32)
    x = jnp.transpose(outputs.astype(jnp.float32), (1, 0, 2)).reshape(seq_len, width)
    part_mean = jnp.mean(x, axis=1, keepdims=True)
    part_dev = x - part_mean
    part_m2 = jnp.sum(jnp.square(part_dev), axis=1, keepdims=True)
    scale_row = lax.dynamic_slice_in_dim(mod_scale, own_clip, 1, axis=0)[0]
    scale_part = lax.dynamic_slice_in_dim(scale_row, own_chunk * width, width)
    weight_part = lax.dynamic_slice_in_dim(weight, own_chunk * width, width, axis=0)
    folded = (1.0 + scale_part)[:, None] * weight_part
    partial = jnp.dot(part_dev, folded, precision=lax.Precision.HIGHEST)
    packed = jnp.concatenate([partial, part_mean, part_m2], axis=1)
    fields = packed.shape[1]
    packed = packed.reshape(n_seq, tok_dev * fields)
    recv = lax.all_to_all(packed, "seq", split_axis=0, concat_axis=0, tiled=True)
    recv = recv.reshape(clips, chunks, tok_dev, fields)
    partials = recv[..., :PATCH_OUT]
    means = recv[..., PATCH_OUT]
    m2s = recv[..., PATCH_OUT + 1]
    mean = jnp.mean(means, axis=1)
    gaps = means - mean[:, None, :]
    m2 = jnp.sum(m2s, axis=1) + width * jnp.sum(jnp.square(gaps), axis=1)
    rstd = lax.rsqrt(m2 / (HEADS * HEAD_DIM) + eps_norm)
    folded_all = jnp.einsum(
        "cjk,jko->cjo",
        (1.0 + mod_scale).reshape(clips, chunks, width),
        weight.reshape(chunks, width, PATCH_OUT),
        precision=lax.Precision.HIGHEST,
    )
    core = jnp.sum(partials, axis=1) + jnp.einsum(
        "cjt,cjo->cto", gaps, folded_all, precision=lax.Precision.HIGHEST
    )
    shift_proj = jnp.dot(mod_shift, weight, precision=lax.Precision.HIGHEST)
    velocity = rstd[..., None] * core + shift_proj[:, None, :] + final_bias
    rows_dev = noisy_latent.shape[2]
    velocity = velocity.reshape(clips, rows_dev // 2, FRAMES, PATCH_W, 2, 2, LAT_CH)
    velocity = jnp.transpose(velocity, (0, 2, 1, 4, 3, 5, 6)).reshape(noisy_latent.shape)
    step = sigma_level(step_index + 1) - sigma_level(step_index)
    denoised = noisy_latent + step[:, None, None, None] * velocity
    decoder_in = denoised.astype(jnp.bfloat16)
    group_index = lax.axis_index(("sec", "rep"))
    wanted = lax.dynamic_slice_in_dim(clip_order, group_index * clips, clips)
    everyone = gather_all(decoder_in, ("sec", "rep"))
    everyone = everyone.reshape((-1,) + decoder_in.shape[1:])
    picked = jnp.take(everyone, wanted, axis=0)
    rimmed = edge_rows(extended(picked, (("seq", 2),), 1))
    grid = rimmed.reshape(clips, FRAMES, rimmed.shape[2], LAT_W, LAT_CH)
    first = grid[:, :1]
    grid = jnp.concatenate([first, first, grid], axis=1)
    grid = jnp.pad(grid, ((0, 0), (0, 0), (0, 0), (1, 1), (0, 0)), mode="edge")
    conv_out = lax.conv_general_dilated(
        grid,
        conv_weight,
        (1, 1, 1),
        "VALID",
        dimension_numbers=("NDHWC", "DHWIO", "NDHWC"),
        preferred_element_type=jnp.float32,
    )
    conv_out = conv_out.reshape(clips, -1, VAE_CH) + conv_bias
    conv_out = conv_out.reshape(clips, -1, GROUPS, VAE_CH // GROUPS)
    count = conv_out.shape[1] * (VAE_CH // GROUPS)
    local_mean = jnp.sum(conv_out, axis=(1, 3)) / count
    centered_local = conv_out - local_mean[:, None, :, None]
    local_m2 = jnp.sum(jnp.square(centered_local), axis=(1, 3))
    moments = gather_all(jnp.stack([local_mean, local_m2]), "seq")
    means, m2s = moments[:, 0], moments[:, 1]
    mean = jnp.mean(means, axis=0)
    m2 = jnp.sum(m2s, axis=0) + count * jnp.sum(jnp.square(means - mean), axis=0)
    centered = conv_out - mean[:, None, :, None]
    spread = m2 / (count * n_seq)
    normed = (centered * lax.rsqrt(spread + eps_norm)[:, None, :, None]).reshape(clips, -1, VAE_CH)
    features = jax.nn.silu(normed * group_gain + group_shift).astype(jnp.bfloat16)
    features = features.reshape(clips, FRAMES, rows_dev, LAT_W * VAE_CH)
    return (denoised, features)


def solution(mesh):
    placed = (
        P(("sec", "rep"), None, "seq", None),
        P(("sec", "rep"), None, "seq", None),
        P(("sec", "rep"), None, "seq", None),
        P(("sec", "rep"), None),
        P(("sec", "rep"), None),
        P(),
        P(),
        P(("sec", "rep"), None, "seq", None),
        P(("sec", "rep")),
        P(),
        P(),
        P(),
        P(),
        P(),
    )
    return jax.shard_map(
        shards,
        mesh=mesh,
        in_specs=placed,
        out_specs=(P(("sec", "rep"), None, "seq", None), P(("sec", "rep"), None, "seq", None)),
        check_vma=False,
    )
```

```python
import math

import jax
import jax.numpy as jnp
from jax import lax
from jax.sharding import PartitionSpec as P

HEADS = 24
HEAD_DIM = 128
LAT_CH = 16
VAE_CH = 512
GROUPS = 32
FRAMES = 3
PATCH_W = 16
NSTEPS = 50
PATCH_OUT = 64
LAT_W = 32


eps_norm = 1e-06
shift_factor = 7.0


def extended(cells, sides, width):
    for axis, dim in sides:
        count = lax.axis_size(axis)
        ends = count - 1
        head = lax.slice_in_dim(cells, 0, width, axis=dim)
        tail = lax.slice_in_dim(cells, cells.shape[dim] - width, cells.shape[dim], axis=dim)
        cells = jnp.concatenate(
            [
                lax.ppermute(tail, axis, [(i, (i + 1) % count) for i in range(ends)]),
                cells,
                lax.ppermute(head, axis, [((i + 1) % count, i) for i in range(ends)]),
            ],
            axis=dim,
        )
    return cells


def gather_all(block, axis):
    count = lax.axis_size(axis)
    copies = jnp.broadcast_to(block[None], (count,) + block.shape)
    return lax.all_to_all(copies, axis, 0, 0, tiled=True)


def butterfly_gather(block, axis):
    count = lax.axis_size(axis)
    me = lax.axis_index(axis)
    held = block[None]
    step = 1
    while step < count:
        other = lax.ppermute(held, axis, [(i, i ^ step) for i in range(count)])
        low = (me // step) % 2 == 0
        held = jnp.where(
            low,
            jnp.concatenate([held, other], axis=0),
            jnp.concatenate([other, held], axis=0),
        )
        step *= 2
    return held.reshape((count * block.shape[0],) + block.shape[1:])


def butterfly_moments(mean, m2, count, axis):
    size = lax.axis_size(axis)
    step = 1
    while step < size:
        pair = lax.ppermute(jnp.stack([mean, m2]), axis, [(i, i ^ step) for i in range(size)])
        other_mean, other_m2 = pair[0], pair[1]
        gap = mean - other_mean
        m2 = (m2 + other_m2) + jnp.square(gap) * (0.5 * count * step)
        mean = (mean + other_mean) * 0.5
        step *= 2
    return mean, m2


def attend_unit(operands):
    query_rows, key_rows, value_rows = operands
    length = query_rows.shape[0]
    block = math.gcd(length, 512)
    scale = 1.0 / math.sqrt(query_rows.shape[1])
    blocks = query_rows.reshape(length // block, block, query_rows.shape[1])

    def one_block(rows):
        scores = jnp.dot(rows, key_rows.T, preferred_element_type=jnp.float32) * scale
        top = jnp.max(scores, axis=1, keepdims=True)
        expd = jnp.exp(scores - top)
        weights = (expd / jnp.sum(expd, axis=1, keepdims=True)).astype(jnp.bfloat16)
        return jnp.dot(weights, value_rows, preferred_element_type=jnp.float32).astype(jnp.bfloat16)

    return lax.map(one_block, blocks).reshape(length, query_rows.shape[1])


def sigma_level(index):
    level = 1.0 - index.astype(jnp.float32) / NSTEPS
    return shift_factor * level / (1.0 + (shift_factor - 1.0) * level)


def causal_columns(rimmed):
    clips, frames, rows_rim, wide = rimmed.shape
    width = wide // LAT_CH
    grid = rimmed.reshape(clips, frames, rows_rim, width, LAT_CH)
    first = grid[:, :1]
    grid = jnp.concatenate([first, first, grid], axis=1)
    grid = jnp.pad(grid, ((0, 0), (0, 0), (0, 0), (1, 1), (0, 0)), mode="edge")
    taps = []
    for tap_time in range(3):
        for tap_row in range(3):
            for tap_col in range(3):
                taps.append(
                    grid[
                        :,
                        tap_time : tap_time + frames,
                        tap_row : tap_row + rows_rim - 2,
                        tap_col : tap_col + width,
                        :,
                    ]
                )
    return jnp.stack(taps, axis=4).reshape(clips, frames, rows_rim - 2, width, 27 * LAT_CH)


def edge_rows(rimmed):
    position = lax.axis_index("seq")
    last_index = lax.axis_size("seq") - 1
    upper = jnp.where(position == 0, rimmed[:, :, 1:2], rimmed[:, :, 0:1])
    lower = jnp.where(position == last_index, rimmed[:, :, -2:-1], rimmed[:, :, -1:])
    return jnp.concatenate([upper, rimmed[:, :, 1:-1], lower], axis=2)


def shards(
    head_query,
    head_keys,
    head_values,
    mod_shift,
    mod_scale,
    final_weight,
    final_bias,
    noisy_latent,
    step_index,
    clip_order,
    conv_weight,
    conv_bias,
    group_gain,
    group_shift,
):
    n_seq = lax.axis_size("seq")
    clips = head_query.shape[0]
    tok_dev = head_query.shape[2]
    units_local = clips * HEADS // n_seq
    stacked = jnp.stack(
        [
            head_query.reshape(n_seq, units_local, tok_dev, HEAD_DIM),
            head_keys.reshape(n_seq, units_local, tok_dev, HEAD_DIM),
            head_values.reshape(n_seq, units_local, tok_dev, HEAD_DIM),
        ],
        axis=1,
    )
    parts = lax.all_to_all(stacked, "seq", split_axis=0, concat_axis=3, tiled=True)
    outputs = lax.map(attend_unit, (parts[0, 0], parts[0, 1], parts[0, 2]))
    seq_len = outputs.shape[1]
    chunks = HEADS // units_local
    width = units_local * HEAD_DIM
    me = lax.axis_index("seq")
    own_clip = me // chunks
    own_chunk = me % chunks
    weight = final_weight.astype(jnp.float32)
    x = jnp.transpose(outputs.astype(jnp.float32), (1, 0, 2)).reshape(seq_len, width)
    part_mean = jnp.mean(x, axis=1, keepdims=True)
    part_dev = x - part_mean
    part_m2 = jnp.sum(jnp.square(part_dev), axis=1, keepdims=True)
    scale_row = lax.dynamic_slice_in_dim(mod_scale, own_clip, 1, axis=0)[0]
    scale_part = lax.dynamic_slice_in_dim(scale_row, own_chunk * width, width)
    weight_part = lax.dynamic_slice_in_dim(weight, own_chunk * width, width, axis=0)
    folded = (1.0 + scale_part)[:, None] * weight_part
    partial = jnp.dot(part_dev, folded, precision=lax.Precision.HIGHEST)
    packed = jnp.concatenate([partial, part_mean, part_m2], axis=1)
    fields = packed.shape[1]
    packed = packed.reshape(n_seq, tok_dev * fields)
    recv = lax.all_to_all(packed, "seq", split_axis=0, concat_axis=0, tiled=True)
    recv = recv.reshape(clips, chunks, tok_dev, fields)
    partials = recv[..., :PATCH_OUT]
    means = recv[..., PATCH_OUT]
    m2s = recv[..., PATCH_OUT + 1]
    mean = jnp.mean(means, axis=1)
    gaps = means - mean[:, None, :]
    m2 = jnp.sum(m2s, axis=1) + width * jnp.sum(jnp.square(gaps), axis=1)
    rstd = lax.rsqrt(m2 / (HEADS * HEAD_DIM) + eps_norm)
    folded_all = jnp.einsum(
        "cjk,jko->cjo",
        (1.0 + mod_scale).reshape(clips, chunks, width),
        weight.reshape(chunks, width, PATCH_OUT),
        precision=lax.Precision.HIGHEST,
    )
    core = jnp.sum(partials, axis=1) + jnp.einsum(
        "cjt,cjo->cto", gaps, folded_all, precision=lax.Precision.HIGHEST
    )
    shift_proj = jnp.dot(mod_shift, weight, precision=lax.Precision.HIGHEST)
    velocity = rstd[..., None] * core + shift_proj[:, None, :] + final_bias
    rows_dev = noisy_latent.shape[2]
    velocity = velocity.reshape(clips, rows_dev // 2, FRAMES, PATCH_W, 2, 2, LAT_CH)
    velocity = jnp.transpose(velocity, (0, 2, 1, 4, 3, 5, 6)).reshape(noisy_latent.shape)
    step = sigma_level(step_index + 1) - sigma_level(step_index)
    denoised = noisy_latent + step[:, None, None, None] * velocity
    decoder_in = denoised.astype(jnp.bfloat16)
    group_index = lax.axis_index(("sec", "rep"))
    wanted = lax.dynamic_slice_in_dim(clip_order, group_index * clips, clips)
    everyone = gather_all(decoder_in, ("sec", "rep"))
    everyone = everyone.reshape((-1,) + decoder_in.shape[1:])
    picked = jnp.take(everyone, wanted, axis=0)
    rimmed = edge_rows(extended(picked, (("seq", 2),), 1))
    grid = rimmed.reshape(clips, FRAMES, rimmed.shape[2], LAT_W, LAT_CH)
    first = grid[:, :1]
    grid = jnp.concatenate([first, first, grid], axis=1)
    grid = jnp.pad(grid, ((0, 0), (0, 0), (0, 0), (1, 1), (0, 0)), mode="edge")
    conv_out = lax.conv_general_dilated(
        grid,
        conv_weight,
        (1, 1, 1),
        "VALID",
        dimension_numbers=("NDHWC", "DHWIO", "NDHWC"),
        preferred_element_type=jnp.float32,
    )
    conv_out = conv_out.reshape(clips, -1, VAE_CH) + conv_bias
    group = VAE_CH // GROUPS
    count = conv_out.shape[1] * group
    chan_sum = jnp.sum(conv_out, axis=1)
    local_mean = jnp.sum(chan_sum.reshape(clips, GROUPS, group), axis=2) / count
    local_mean_c = jnp.repeat(local_mean, group, axis=1)
    chan_m2 = jnp.sum(jnp.square(conv_out - local_mean_c[:, None, :]), axis=1)
    local_m2 = jnp.sum(chan_m2.reshape(clips, GROUPS, group), axis=2)
    moments = gather_all(jnp.stack([local_mean, local_m2]), "seq")
    means, m2s = moments[:, 0], moments[:, 1]
    mean = jnp.mean(means, axis=0)
    m2 = jnp.sum(m2s, axis=0) + count * jnp.sum(jnp.square(means - mean), axis=0)
    spread = m2 / (count * n_seq)
    mean_c = jnp.repeat(mean, group, axis=1)
    factor_c = jnp.repeat(lax.rsqrt(spread + eps_norm), group, axis=1) * group_gain
    features = jax.nn.silu(
        (conv_out - mean_c[:, None, :]) * factor_c[:, None, :] + group_shift
    ).astype(jnp.bfloat16)
    features = features.reshape(clips, FRAMES, rows_dev, LAT_W * VAE_CH)
    return (denoised, features)


def solution(mesh):
    placed = (
        P(("sec", "rep"), None, "seq", None),
        P(("sec", "rep"), None, "seq", None),
        P(("sec", "rep"), None, "seq", None),
        P(("sec", "rep"), None),
        P(("sec", "rep"), None),
        P(),
        P(),
        P(("sec", "rep"), None, "seq", None),
        P(("sec", "rep")),
        P(),
        P(),
        P(),
        P(),
        P(),
    )
    return jax.shard_map(
        shards,
        mesh=mesh,
        in_specs=placed,
        out_specs=(P(("sec", "rep"), None, "seq", None), P(("sec", "rep"), None, "seq", None)),
        check_vma=False,
    )
```

```python
import math

import jax
import jax.numpy as jnp
from jax import lax
from jax.sharding import PartitionSpec as P

HEADS = 24
HEAD_DIM = 128
LAT_CH = 16
VAE_CH = 512
GROUPS = 32
FRAMES = 3
PATCH_W = 16
NSTEPS = 50
PATCH_OUT = 64
LAT_W = 32


eps_norm = 1e-06
shift_factor = 7.0


def extended(cells, sides, width):
    for axis, dim in sides:
        count = lax.axis_size(axis)
        ends = count - 1
        head = lax.slice_in_dim(cells, 0, width, axis=dim)
        tail = lax.slice_in_dim(cells, cells.shape[dim] - width, cells.shape[dim], axis=dim)
        cells = jnp.concatenate(
            [
                lax.ppermute(tail, axis, [(i, (i + 1) % count) for i in range(ends)]),
                cells,
                lax.ppermute(head, axis, [((i + 1) % count, i) for i in range(ends)]),
            ],
            axis=dim,
        )
    return cells


def gather_all(block, axis):
    count = lax.axis_size(axis)
    copies = jnp.broadcast_to(block[None], (count,) + block.shape)
    return lax.all_to_all(copies, axis, 0, 0, tiled=True)


def butterfly_gather(block, axis):
    count = lax.axis_size(axis)
    me = lax.axis_index(axis)
    held = block[None]
    step = 1
    while step < count:
        other = lax.ppermute(held, axis, [(i, i ^ step) for i in range(count)])
        low = (me // step) % 2 == 0
        held = jnp.where(
            low,
            jnp.concatenate([held, other], axis=0),
            jnp.concatenate([other, held], axis=0),
        )
        step *= 2
    return held.reshape((count * block.shape[0],) + block.shape[1:])


def butterfly_moments(mean, m2, count, axis):
    size = lax.axis_size(axis)
    step = 1
    while step < size:
        pair = lax.ppermute(jnp.stack([mean, m2]), axis, [(i, i ^ step) for i in range(size)])
        other_mean, other_m2 = pair[0], pair[1]
        gap = mean - other_mean
        m2 = (m2 + other_m2) + jnp.square(gap) * (0.5 * count * step)
        mean = (mean + other_mean) * 0.5
        step *= 2
    return mean, m2


def attend_unit(operands):
    query_rows, key_rows, value_rows = operands
    length = query_rows.shape[0]
    block = math.gcd(length, 512)
    scale = 1.0 / math.sqrt(query_rows.shape[1])
    blocks = query_rows.reshape(length // block, block, query_rows.shape[1])

    def one_block(rows):
        scores = jnp.dot(rows, key_rows.T, preferred_element_type=jnp.float32) * scale
        top = jnp.max(scores, axis=1, keepdims=True)
        expd = jnp.exp(scores - top)
        weights = (expd / jnp.sum(expd, axis=1, keepdims=True)).astype(jnp.bfloat16)
        return jnp.dot(weights, value_rows, preferred_element_type=jnp.float32).astype(jnp.bfloat16)

    return lax.map(one_block, blocks).reshape(length, query_rows.shape[1])


def sigma_level(index):
    level = 1.0 - index.astype(jnp.float32) / NSTEPS
    return shift_factor * level / (1.0 + (shift_factor - 1.0) * level)


def causal_columns(rimmed):
    clips, frames, rows_rim, wide = rimmed.shape
    width = wide // LAT_CH
    grid = rimmed.reshape(clips, frames, rows_rim, width, LAT_CH)
    first = grid[:, :1]
    grid = jnp.concatenate([first, first, grid], axis=1)
    grid = jnp.pad(grid, ((0, 0), (0, 0), (0, 0), (1, 1), (0, 0)), mode="edge")
    taps = []
    for tap_time in range(3):
        for tap_row in range(3):
            for tap_col in range(3):
                taps.append(
                    grid[
                        :,
                        tap_time : tap_time + frames,
                        tap_row : tap_row + rows_rim - 2,
                        tap_col : tap_col + width,
                        :,
                    ]
                )
    return jnp.stack(taps, axis=4).reshape(clips, frames, rows_rim - 2, width, 27 * LAT_CH)


def edge_rows(rimmed):
    position = lax.axis_index("seq")
    last_index = lax.axis_size("seq") - 1
    upper = jnp.where(position == 0, rimmed[:, :, 1:2], rimmed[:, :, 0:1])
    lower = jnp.where(position == last_index, rimmed[:, :, -2:-1], rimmed[:, :, -1:])
    return jnp.concatenate([upper, rimmed[:, :, 1:-1], lower], axis=2)


def shards(
    head_query,
    head_keys,
    head_values,
    mod_shift,
    mod_scale,
    final_weight,
    final_bias,
    noisy_latent,
    step_index,
    clip_order,
    conv_weight,
    conv_bias,
    group_gain,
    group_shift,
):
    n_seq = lax.axis_size("seq")
    clips = head_query.shape[0]
    tok_dev = head_query.shape[2]
    units_local = clips * HEADS // n_seq
    stacked = jnp.stack(
        [
            head_query.reshape(n_seq, units_local, tok_dev, HEAD_DIM),
            head_keys.reshape(n_seq, units_local, tok_dev, HEAD_DIM),
            head_values.reshape(n_seq, units_local, tok_dev, HEAD_DIM),
        ],
        axis=1,
    )
    parts = lax.all_to_all(stacked, "seq", split_axis=0, concat_axis=3, tiled=True)
    outputs = lax.map(attend_unit, (parts[0, 0], parts[0, 1], parts[0, 2]))
    seq_len = outputs.shape[1]
    chunks = HEADS // units_local
    width = units_local * HEAD_DIM
    me = lax.axis_index("seq")
    own_clip = me // chunks
    own_chunk = me % chunks
    weight = final_weight.astype(jnp.float32)
    x = jnp.transpose(outputs.astype(jnp.float32), (1, 0, 2)).reshape(seq_len, width)
    part_mean = jnp.mean(x, axis=1, keepdims=True)
    part_dev = x - part_mean
    part_m2 = jnp.sum(jnp.square(part_dev), axis=1, keepdims=True)
    scale_row = lax.dynamic_slice_in_dim(mod_scale, own_clip, 1, axis=0)[0]
    scale_part = lax.dynamic_slice_in_dim(scale_row, own_chunk * width, width)
    weight_part = lax.dynamic_slice_in_dim(weight, own_chunk * width, width, axis=0)
    folded = (1.0 + scale_part)[:, None] * weight_part
    partial = jnp.dot(part_dev, folded, precision=lax.Precision.HIGHEST)
    packed = jnp.concatenate([partial, part_mean, part_m2], axis=1)
    fields = packed.shape[1]
    packed = packed.reshape(n_seq, tok_dev * fields)
    recv = lax.all_to_all(packed, "seq", split_axis=0, concat_axis=0, tiled=True)
    recv = recv.reshape(clips, chunks, tok_dev, fields)
    partials = recv[..., :PATCH_OUT]
    means = recv[..., PATCH_OUT]
    m2s = recv[..., PATCH_OUT + 1]
    mean = jnp.mean(means, axis=1)
    gaps = means - mean[:, None, :]
    m2 = jnp.sum(m2s, axis=1) + width * jnp.sum(jnp.square(gaps), axis=1)
    rstd = lax.rsqrt(m2 / (HEADS * HEAD_DIM) + eps_norm)
    folded_all = jnp.einsum(
        "cjk,jko->cjo",
        (1.0 + mod_scale).reshape(clips, chunks, width),
        weight.reshape(chunks, width, PATCH_OUT),
        precision=lax.Precision.HIGHEST,
    )
    core = jnp.sum(partials, axis=1) + jnp.einsum(
        "cjt,cjo->cto", gaps, folded_all, precision=lax.Precision.HIGHEST
    )
    shift_proj = jnp.dot(mod_shift, weight, precision=lax.Precision.HIGHEST)
    velocity = rstd[..., None] * core + shift_proj[:, None, :] + final_bias
    rows_dev = noisy_latent.shape[2]
    velocity = velocity.reshape(clips, rows_dev // 2, FRAMES, PATCH_W, 2, 2, LAT_CH)
    velocity = jnp.transpose(velocity, (0, 2, 1, 4, 3, 5, 6)).reshape(noisy_latent.shape)
    step = sigma_level(step_index + 1) - sigma_level(step_index)
    denoised = noisy_latent + step[:, None, None, None] * velocity
    decoder_in = denoised.astype(jnp.bfloat16)
    group_index = lax.axis_index(("sec", "rep"))
    wanted = lax.dynamic_slice_in_dim(clip_order, group_index * clips, clips)
    everyone = gather_all(decoder_in, ("sec", "rep"))
    everyone = everyone.reshape((-1,) + decoder_in.shape[1:])
    picked = jnp.take(everyone, wanted, axis=0)
    rimmed = edge_rows(extended(picked, (("seq", 2),), 1))
    grid = rimmed.reshape(clips, FRAMES, rimmed.shape[2], LAT_W, LAT_CH)
    first = grid[:, :1]
    grid = jnp.concatenate([first, first, grid], axis=1)
    grid = jnp.pad(grid, ((0, 0), (0, 0), (0, 0), (1, 1), (0, 0)), mode="edge")
    conv_out = lax.conv_general_dilated(
        grid,
        conv_weight,
        (1, 1, 1),
        "VALID",
        dimension_numbers=("NDHWC", "DHWIO", "NDHWC"),
        preferred_element_type=jnp.float32,
    )
    conv_out = conv_out.reshape(clips, -1, VAE_CH) + conv_bias
    group = VAE_CH // GROUPS
    count = conv_out.shape[1] * group
    chan_sum = jnp.sum(conv_out, axis=1)
    local_mean = jnp.sum(chan_sum.reshape(clips, GROUPS, group), axis=2) / count
    local_mean_c = jnp.repeat(local_mean, group, axis=1)
    chan_m2 = jnp.sum(jnp.square(conv_out - local_mean_c[:, None, :]), axis=1)
    local_m2 = jnp.sum(chan_m2.reshape(clips, GROUPS, group), axis=2)
    moments = gather_all(jnp.stack([local_mean, local_m2]), "seq")
    means, m2s = moments[:, 0], moments[:, 1]
    mean = jnp.mean(means, axis=0)
    m2 = jnp.sum(m2s, axis=0) + count * jnp.sum(jnp.square(means - mean), axis=0)
    spread = m2 / (count * n_seq)
    mean_c = jnp.repeat(mean, group, axis=1)
    factor_c = jnp.repeat(lax.rsqrt(spread + eps_norm), group, axis=1) * group_gain
    laid = conv_out.reshape(clips, FRAMES, rows_dev, LAT_W * VAE_CH)
    mean_t = jnp.tile(mean_c, (1, LAT_W))[:, None, None, :]
    factor_t = jnp.tile(factor_c, (1, LAT_W))[:, None, None, :]
    shift_t = jnp.tile(group_shift, LAT_W)
    features = jax.nn.silu((laid - mean_t) * factor_t + shift_t).astype(jnp.bfloat16)
    return (denoised, features)


def solution(mesh):
    placed = (
        P(("sec", "rep"), None, "seq", None),
        P(("sec", "rep"), None, "seq", None),
        P(("sec", "rep"), None, "seq", None),
        P(("sec", "rep"), None),
        P(("sec", "rep"), None),
        P(),
        P(),
        P(("sec", "rep"), None, "seq", None),
        P(("sec", "rep")),
        P(),
        P(),
        P(),
        P(),
        P(),
    )
    return jax.shard_map(
        shards,
        mesh=mesh,
        in_specs=placed,
        out_specs=(P(("sec", "rep"), None, "seq", None), P(("sec", "rep"), None, "seq", None)),
        check_vma=False,
    )
```

```python
import math

import jax
import jax.numpy as jnp
from jax import lax
from jax.experimental import pallas as pl
from jax.sharding import PartitionSpec as P

HEADS = 24
HEAD_DIM = 128
LAT_CH = 16
VAE_CH = 512
GROUPS = 32
FRAMES = 3
PATCH_W = 16
NSTEPS = 50
PATCH_OUT = 64
LAT_W = 32


eps_norm = 1e-06
shift_factor = 7.0


def extended(cells, sides, width):
    for axis, dim in sides:
        count = lax.axis_size(axis)
        ends = count - 1
        head = lax.slice_in_dim(cells, 0, width, axis=dim)
        tail = lax.slice_in_dim(cells, cells.shape[dim] - width, cells.shape[dim], axis=dim)
        cells = jnp.concatenate(
            [
                lax.ppermute(tail, axis, [(i, (i + 1) % count) for i in range(ends)]),
                cells,
                lax.ppermute(head, axis, [((i + 1) % count, i) for i in range(ends)]),
            ],
            axis=dim,
        )
    return cells


def gather_all(block, axis):
    count = lax.axis_size(axis)
    copies = jnp.broadcast_to(block[None], (count,) + block.shape)
    return lax.all_to_all(copies, axis, 0, 0, tiled=True)


def butterfly_gather(block, axis):
    count = lax.axis_size(axis)
    me = lax.axis_index(axis)
    held = block[None]
    step = 1
    while step < count:
        other = lax.ppermute(held, axis, [(i, i ^ step) for i in range(count)])
        low = (me // step) % 2 == 0
        held = jnp.where(
            low,
            jnp.concatenate([held, other], axis=0),
            jnp.concatenate([other, held], axis=0),
        )
        step *= 2
    return held.reshape((count * block.shape[0],) + block.shape[1:])


def butterfly_moments(mean, m2, count, axis):
    size = lax.axis_size(axis)
    step = 1
    while step < size:
        pair = lax.ppermute(jnp.stack([mean, m2]), axis, [(i, i ^ step) for i in range(size)])
        other_mean, other_m2 = pair[0], pair[1]
        gap = mean - other_mean
        m2 = (m2 + other_m2) + jnp.square(gap) * (0.5 * count * step)
        mean = (mean + other_mean) * 0.5
        step *= 2
    return mean, m2


QUERY_BLOCK = 512

def attend_kernel(scale, q_ref, k_ref, v_ref, o_ref):
    scores = lax.dot_general(
        q_ref[0], k_ref[0], (((1,), (1,)), ((), ())), preferred_element_type=jnp.float32
    ) * scale
    top = jnp.max(scores, axis=1, keepdims=True)
    expd = jnp.exp(scores - top)
    weights = (expd / jnp.sum(expd, axis=1, keepdims=True)).astype(jnp.bfloat16)
    o_ref[0] = jnp.dot(weights, v_ref[0], preferred_element_type=jnp.float32).astype(o_ref.dtype)

def attend_units(query, keys, values):
    units, length, depth = query.shape
    block = math.gcd(length, QUERY_BLOCK)
    scale = 1.0 / math.sqrt(depth)
    return pl.pallas_call(
        lambda *refs: attend_kernel(scale, *refs),
        grid=(units, length // block),
        in_specs=[
            pl.BlockSpec((1, block, depth), lambda u, b: (u, b, 0)),
            pl.BlockSpec((1, length, depth), lambda u, b: (u, 0, 0)),
            pl.BlockSpec((1, length, depth), lambda u, b: (u, 0, 0)),
        ],
        out_specs=pl.BlockSpec((1, block, depth), lambda u, b: (u, b, 0)),
        out_shape=jax.ShapeDtypeStruct((units, length, depth), jnp.bfloat16),
        cost_estimate=pl.CostEstimate(
            flops=4 * units * length * length * depth,
            transcendentals=units * length * length,
            bytes_accessed=4 * units * length * depth * 2,
        ),
    )(query, keys, values)


def attend_unit(operands):
    query_rows, key_rows, value_rows = operands
    length = query_rows.shape[0]
    block = math.gcd(length, 512)
    scale = 1.0 / math.sqrt(query_rows.shape[1])
    blocks = query_rows.reshape(length // block, block, query_rows.shape[1])

    def one_block(rows):
        scores = jnp.dot(rows, key_rows.T, preferred_element_type=jnp.float32) * scale
        top = jnp.max(scores, axis=1, keepdims=True)
        expd = jnp.exp(scores - top)
        weights = (expd / jnp.sum(expd, axis=1, keepdims=True)).astype(jnp.bfloat16)
        return jnp.dot(weights, value_rows, preferred_element_type=jnp.float32).astype(jnp.bfloat16)

    return lax.map(one_block, blocks).reshape(length, query_rows.shape[1])


def sigma_level(index):
    level = 1.0 - index.astype(jnp.float32) / NSTEPS
    return shift_factor * level / (1.0 + (shift_factor - 1.0) * level)


def causal_columns(rimmed):
    clips, frames, rows_rim, wide = rimmed.shape
    width = wide // LAT_CH
    grid = rimmed.reshape(clips, frames, rows_rim, width, LAT_CH)
    first = grid[:, :1]
    grid = jnp.concatenate([first, first, grid], axis=1)
    grid = jnp.pad(grid, ((0, 0), (0, 0), (0, 0), (1, 1), (0, 0)), mode="edge")
    taps = []
    for tap_time in range(3):
        for tap_row in range(3):
            for tap_col in range(3):
                taps.append(
                    grid[
                        :,
                        tap_time : tap_time + frames,
                        tap_row : tap_row + rows_rim - 2,
                        tap_col : tap_col + width,
                        :,
                    ]
                )
    return jnp.stack(taps, axis=4).reshape(clips, frames, rows_rim - 2, width, 27 * LAT_CH)


def edge_rows(rimmed):
    position = lax.axis_index("seq")
    last_index = lax.axis_size("seq") - 1
    upper = jnp.where(position == 0, rimmed[:, :, 1:2], rimmed[:, :, 0:1])
    lower = jnp.where(position == last_index, rimmed[:, :, -2:-1], rimmed[:, :, -1:])
    return jnp.concatenate([upper, rimmed[:, :, 1:-1], lower], axis=2)


def shards(
    head_query,
    head_keys,
    head_values,
    mod_shift,
    mod_scale,
    final_weight,
    final_bias,
    noisy_latent,
    step_index,
    clip_order,
    conv_weight,
    conv_bias,
    group_gain,
    group_shift,
):
    n_seq = lax.axis_size("seq")
    clips = head_query.shape[0]
    tok_dev = head_query.shape[2]
    units_local = clips * HEADS // n_seq
    stacked = jnp.stack(
        [
            head_query.reshape(n_seq, units_local, tok_dev, HEAD_DIM),
            head_keys.reshape(n_seq, units_local, tok_dev, HEAD_DIM),
            head_values.reshape(n_seq, units_local, tok_dev, HEAD_DIM),
        ],
        axis=1,
    )
    parts = lax.all_to_all(stacked, "seq", split_axis=0, concat_axis=3, tiled=True)
    outputs = attend_units(parts[0, 0], parts[0, 1], parts[0, 2])
    seq_len = outputs.shape[1]
    chunks = HEADS // units_local
    width = units_local * HEAD_DIM
    me = lax.axis_index("seq")
    own_clip = me // chunks
    own_chunk = me % chunks
    weight = final_weight.astype(jnp.float32)
    x = jnp.transpose(outputs.astype(jnp.float32), (1, 0, 2)).reshape(seq_len, width)
    part_mean = jnp.mean(x, axis=1, keepdims=True)
    part_dev = x - part_mean
    part_m2 = jnp.sum(jnp.square(part_dev), axis=1, keepdims=True)
    scale_row = lax.dynamic_slice_in_dim(mod_scale, own_clip, 1, axis=0)[0]
    scale_part = lax.dynamic_slice_in_dim(scale_row, own_chunk * width, width)
    weight_part = lax.dynamic_slice_in_dim(weight, own_chunk * width, width, axis=0)
    folded = (1.0 + scale_part)[:, None] * weight_part
    partial = jnp.dot(part_dev, folded, precision=lax.Precision.HIGHEST)
    packed = jnp.concatenate([partial, part_mean, part_m2], axis=1)
    fields = packed.shape[1]
    packed = packed.reshape(n_seq, tok_dev * fields)
    recv = lax.all_to_all(packed, "seq", split_axis=0, concat_axis=0, tiled=True)
    recv = recv.reshape(clips, chunks, tok_dev, fields)
    partials = recv[..., :PATCH_OUT]
    means = recv[..., PATCH_OUT]
    m2s = recv[..., PATCH_OUT + 1]
    mean = jnp.mean(means, axis=1)
    gaps = means - mean[:, None, :]
    m2 = jnp.sum(m2s, axis=1) + width * jnp.sum(jnp.square(gaps), axis=1)
    rstd = lax.rsqrt(m2 / (HEADS * HEAD_DIM) + eps_norm)
    folded_all = jnp.einsum(
        "cjk,jko->cjo",
        (1.0 + mod_scale).reshape(clips, chunks, width),
        weight.reshape(chunks, width, PATCH_OUT),
        precision=lax.Precision.HIGHEST,
    )
    core = jnp.sum(partials, axis=1) + jnp.einsum(
        "cjt,cjo->cto", gaps, folded_all, precision=lax.Precision.HIGHEST
    )
    shift_proj = jnp.dot(mod_shift, weight, precision=lax.Precision.HIGHEST)
    velocity = rstd[..., None] * core + shift_proj[:, None, :] + final_bias
    rows_dev = noisy_latent.shape[2]
    velocity = velocity.reshape(clips, rows_dev // 2, FRAMES, PATCH_W, 2, 2, LAT_CH)
    velocity = jnp.transpose(velocity, (0, 2, 1, 4, 3, 5, 6)).reshape(noisy_latent.shape)
    step = sigma_level(step_index + 1) - sigma_level(step_index)
    denoised = noisy_latent + step[:, None, None, None] * velocity
    decoder_in = denoised.astype(jnp.bfloat16)
    group_index = lax.axis_index(("sec", "rep"))
    wanted = lax.dynamic_slice_in_dim(clip_order, group_index * clips, clips)
    everyone = gather_all(decoder_in, ("sec", "rep"))
    everyone = everyone.reshape((-1,) + decoder_in.shape[1:])
    picked = jnp.take(everyone, wanted, axis=0)
    rimmed = edge_rows(extended(picked, (("seq", 2),), 1))
    grid = rimmed.reshape(clips, FRAMES, rimmed.shape[2], LAT_W, LAT_CH)
    first = grid[:, :1]
    grid = jnp.concatenate([first, first, grid], axis=1)
    grid = jnp.pad(grid, ((0, 0), (0, 0), (0, 0), (1, 1), (0, 0)), mode="edge")
    conv_out = lax.conv_general_dilated(
        grid,
        conv_weight,
        (1, 1, 1),
        "VALID",
        dimension_numbers=("NDHWC", "DHWIO", "NDHWC"),
        preferred_element_type=jnp.float32,
    )
    conv_out = conv_out.reshape(clips, -1, VAE_CH) + conv_bias
    group = VAE_CH // GROUPS
    count = conv_out.shape[1] * group
    chan_sum = jnp.sum(conv_out, axis=1)
    local_mean = jnp.sum(chan_sum.reshape(clips, GROUPS, group), axis=2) / count
    local_mean_c = jnp.repeat(local_mean, group, axis=1)
    chan_m2 = jnp.sum(jnp.square(conv_out - local_mean_c[:, None, :]), axis=1)
    local_m2 = jnp.sum(chan_m2.reshape(clips, GROUPS, group), axis=2)
    moments = gather_all(jnp.stack([local_mean, local_m2]), "seq")
    means, m2s = moments[:, 0], moments[:, 1]
    mean = jnp.mean(means, axis=0)
    m2 = jnp.sum(m2s, axis=0) + count * jnp.sum(jnp.square(means - mean), axis=0)
    spread = m2 / (count * n_seq)
    mean_c = jnp.repeat(mean, group, axis=1)
    factor_c = jnp.repeat(lax.rsqrt(spread + eps_norm), group, axis=1) * group_gain
    laid = conv_out.reshape(clips, FRAMES, rows_dev, LAT_W * VAE_CH)
    mean_t = jnp.tile(mean_c, (1, LAT_W))[:, None, None, :]
    factor_t = jnp.tile(factor_c, (1, LAT_W))[:, None, None, :]
    shift_t = jnp.tile(group_shift, LAT_W)
    features = jax.nn.silu((laid - mean_t) * factor_t + shift_t).astype(jnp.bfloat16)
    return (denoised, features)


def solution(mesh):
    placed = (
        P(("sec", "rep"), None, "seq", None),
        P(("sec", "rep"), None, "seq", None),
        P(("sec", "rep"), None, "seq", None),
        P(("sec", "rep"), None),
        P(("sec", "rep"), None),
        P(),
        P(),
        P(("sec", "rep"), None, "seq", None),
        P(("sec", "rep")),
        P(),
        P(),
        P(),
        P(),
        P(),
    )
    return jax.shard_map(
        shards,
        mesh=mesh,
        in_specs=placed,
        out_specs=(P(("sec", "rep"), None, "seq", None), P(("sec", "rep"), None, "seq", None)),
        check_vma=False,
    )
```

```python
import math

import jax
import jax.numpy as jnp
from jax import lax
from jax.sharding import PartitionSpec as P

HEADS = 24
HEAD_DIM = 128
LAT_CH = 16
VAE_CH = 512
GROUPS = 32
FRAMES = 3
PATCH_W = 16
NSTEPS = 50
PATCH_OUT = 64
LAT_W = 32


eps_norm = 1e-06
shift_factor = 7.0


def extended(cells, sides, width):
    for axis, dim in sides:
        count = lax.axis_size(axis)
        ends = count - 1
        head = lax.slice_in_dim(cells, 0, width, axis=dim)
        tail = lax.slice_in_dim(cells, cells.shape[dim] - width, cells.shape[dim], axis=dim)
        cells = jnp.concatenate(
            [
                lax.ppermute(tail, axis, [(i, (i + 1) % count) for i in range(ends)]),
                cells,
                lax.ppermute(head, axis, [((i + 1) % count, i) for i in range(ends)]),
            ],
            axis=dim,
        )
    return cells


def gather_all(block, axis):
    count = lax.axis_size(axis)
    copies = jnp.broadcast_to(block[None], (count,) + block.shape)
    return lax.all_to_all(copies, axis, 0, 0, tiled=True)


def butterfly_gather(block, axis):
    count = lax.axis_size(axis)
    me = lax.axis_index(axis)
    held = block[None]
    step = 1
    while step < count:
        other = lax.ppermute(held, axis, [(i, i ^ step) for i in range(count)])
        low = (me // step) % 2 == 0
        held = jnp.where(
            low,
            jnp.concatenate([held, other], axis=0),
            jnp.concatenate([other, held], axis=0),
        )
        step *= 2
    return held.reshape((count * block.shape[0],) + block.shape[1:])


def butterfly_moments(mean, m2, count, axis):
    size = lax.axis_size(axis)
    step = 1
    while step < size:
        pair = lax.ppermute(jnp.stack([mean, m2]), axis, [(i, i ^ step) for i in range(size)])
        other_mean, other_m2 = pair[0], pair[1]
        gap = mean - other_mean
        m2 = (m2 + other_m2) + jnp.square(gap) * (0.5 * count * step)
        mean = (mean + other_mean) * 0.5
        step *= 2
    return mean, m2


def attend_unit(operands):
    query_rows, key_rows, value_rows = operands
    length = query_rows.shape[0]
    block = length
    scale = 1.0 / math.sqrt(query_rows.shape[1])
    blocks = query_rows.reshape(length // block, block, query_rows.shape[1])

    def one_block(rows):
        scores = jnp.dot(rows, key_rows.T, preferred_element_type=jnp.float32) * scale
        top = jnp.max(scores, axis=1, keepdims=True)
        expd = jnp.exp(scores - top)
        weights = (expd / jnp.sum(expd, axis=1, keepdims=True)).astype(jnp.bfloat16)
        return jnp.dot(weights, value_rows, preferred_element_type=jnp.float32).astype(jnp.bfloat16)

    return lax.map(one_block, blocks).reshape(length, query_rows.shape[1])


def sigma_level(index):
    level = 1.0 - index.astype(jnp.float32) / NSTEPS
    return shift_factor * level / (1.0 + (shift_factor - 1.0) * level)


def causal_columns(rimmed):
    clips, frames, rows_rim, wide = rimmed.shape
    width = wide // LAT_CH
    grid = rimmed.reshape(clips, frames, rows_rim, width, LAT_CH)
    first = grid[:, :1]
    grid = jnp.concatenate([first, first, grid], axis=1)
    grid = jnp.pad(grid, ((0, 0), (0, 0), (0, 0), (1, 1), (0, 0)), mode="edge")
    taps = []
    for tap_time in range(3):
        for tap_row in range(3):
            for tap_col in range(3):
                taps.append(
                    grid[
                        :,
                        tap_time : tap_time + frames,
                        tap_row : tap_row + rows_rim - 2,
                        tap_col : tap_col + width,
                        :,
                    ]
                )
    return jnp.stack(taps, axis=4).reshape(clips, frames, rows_rim - 2, width, 27 * LAT_CH)


def edge_rows(rimmed):
    position = lax.axis_index("seq")
    last_index = lax.axis_size("seq") - 1
    upper = jnp.where(position == 0, rimmed[:, :, 1:2], rimmed[:, :, 0:1])
    lower = jnp.where(position == last_index, rimmed[:, :, -2:-1], rimmed[:, :, -1:])
    return jnp.concatenate([upper, rimmed[:, :, 1:-1], lower], axis=2)


def shards(
    head_query,
    head_keys,
    head_values,
    mod_shift,
    mod_scale,
    final_weight,
    final_bias,
    noisy_latent,
    step_index,
    clip_order,
    conv_weight,
    conv_bias,
    group_gain,
    group_shift,
):
    n_seq = lax.axis_size("seq")
    clips = head_query.shape[0]
    tok_dev = head_query.shape[2]
    units_local = clips * HEADS // n_seq
    stacked = jnp.stack(
        [
            head_query.reshape(n_seq, units_local, tok_dev, HEAD_DIM),
            head_keys.reshape(n_seq, units_local, tok_dev, HEAD_DIM),
            head_values.reshape(n_seq, units_local, tok_dev, HEAD_DIM),
        ],
        axis=1,
    )
    parts = lax.all_to_all(stacked, "seq", split_axis=0, concat_axis=3, tiled=True)
    outputs = lax.map(attend_unit, (parts[0, 0], parts[0, 1], parts[0, 2]))
    seq_len = outputs.shape[1]
    chunks = HEADS // units_local
    width = units_local * HEAD_DIM
    me = lax.axis_index("seq")
    own_clip = me // chunks
    own_chunk = me % chunks
    weight = final_weight.astype(jnp.float32)
    x = jnp.transpose(outputs.astype(jnp.float32), (1, 0, 2)).reshape(seq_len, width)
    part_mean = jnp.mean(x, axis=1, keepdims=True)
    part_dev = x - part_mean
    part_m2 = jnp.sum(jnp.square(part_dev), axis=1, keepdims=True)
    scale_row = lax.dynamic_slice_in_dim(mod_scale, own_clip, 1, axis=0)[0]
    scale_part = lax.dynamic_slice_in_dim(scale_row, own_chunk * width, width)
    weight_part = lax.dynamic_slice_in_dim(weight, own_chunk * width, width, axis=0)
    folded = (1.0 + scale_part)[:, None] * weight_part
    partial = jnp.dot(part_dev, folded, precision=lax.Precision.HIGHEST)
    packed = jnp.concatenate([partial, part_mean, part_m2], axis=1)
    fields = packed.shape[1]
    packed = packed.reshape(n_seq, tok_dev * fields)
    recv = lax.all_to_all(packed, "seq", split_axis=0, concat_axis=0, tiled=True)
    recv = recv.reshape(clips, chunks, tok_dev, fields)
    partials = recv[..., :PATCH_OUT]
    means = recv[..., PATCH_OUT]
    m2s = recv[..., PATCH_OUT + 1]
    mean = jnp.mean(means, axis=1)
    gaps = means - mean[:, None, :]
    m2 = jnp.sum(m2s, axis=1) + width * jnp.sum(jnp.square(gaps), axis=1)
    rstd = lax.rsqrt(m2 / (HEADS * HEAD_DIM) + eps_norm)
    folded_all = jnp.einsum(
        "cjk,jko->cjo",
        (1.0 + mod_scale).reshape(clips, chunks, width),
        weight.reshape(chunks, width, PATCH_OUT),
        precision=lax.Precision.HIGHEST,
    )
    core = jnp.sum(partials, axis=1) + jnp.einsum(
        "cjt,cjo->cto", gaps, folded_all, precision=lax.Precision.HIGHEST
    )
    shift_proj = jnp.dot(mod_shift, weight, precision=lax.Precision.HIGHEST)
    velocity = rstd[..., None] * core + shift_proj[:, None, :] + final_bias
    rows_dev = noisy_latent.shape[2]
    velocity = velocity.reshape(clips, rows_dev // 2, FRAMES, PATCH_W, 2, 2, LAT_CH)
    velocity = jnp.transpose(velocity, (0, 2, 1, 4, 3, 5, 6)).reshape(noisy_latent.shape)
    step = sigma_level(step_index + 1) - sigma_level(step_index)
    denoised = noisy_latent + step[:, None, None, None] * velocity
    decoder_in = denoised.astype(jnp.bfloat16)
    group_index = lax.axis_index(("sec", "rep"))
    wanted = lax.dynamic_slice_in_dim(clip_order, group_index * clips, clips)
    everyone = gather_all(decoder_in, ("sec", "rep"))
    everyone = everyone.reshape((-1,) + decoder_in.shape[1:])
    picked = jnp.take(everyone, wanted, axis=0)
    rimmed = edge_rows(extended(picked, (("seq", 2),), 1))
    grid = rimmed.reshape(clips, FRAMES, rimmed.shape[2], LAT_W, LAT_CH)
    first = grid[:, :1]
    grid = jnp.concatenate([first, first, grid], axis=1)
    grid = jnp.pad(grid, ((0, 0), (0, 0), (0, 0), (1, 1), (0, 0)), mode="edge")
    conv_out = lax.conv_general_dilated(
        grid,
        conv_weight,
        (1, 1, 1),
        "VALID",
        dimension_numbers=("NDHWC", "DHWIO", "NDHWC"),
        preferred_element_type=jnp.float32,
    )
    conv_out = conv_out.reshape(clips, -1, VAE_CH) + conv_bias
    group = VAE_CH // GROUPS
    count = conv_out.shape[1] * group
    chan_sum = jnp.sum(conv_out, axis=1)
    local_mean = jnp.sum(chan_sum.reshape(clips, GROUPS, group), axis=2) / count
    local_mean_c = jnp.repeat(local_mean, group, axis=1)
    chan_m2 = jnp.sum(jnp.square(conv_out - local_mean_c[:, None, :]), axis=1)
    local_m2 = jnp.sum(chan_m2.reshape(clips, GROUPS, group), axis=2)
    moments = gather_all(jnp.stack([local_mean, local_m2]), "seq")
    means, m2s = moments[:, 0], moments[:, 1]
    mean = jnp.mean(means, axis=0)
    m2 = jnp.sum(m2s, axis=0) + count * jnp.sum(jnp.square(means - mean), axis=0)
    spread = m2 / (count * n_seq)
    mean_c = jnp.repeat(mean, group, axis=1)
    factor_c = jnp.repeat(lax.rsqrt(spread + eps_norm), group, axis=1) * group_gain
    laid = conv_out.reshape(clips, FRAMES, rows_dev, LAT_W * VAE_CH)
    mean_t = jnp.tile(mean_c, (1, LAT_W))[:, None, None, :]
    factor_t = jnp.tile(factor_c, (1, LAT_W))[:, None, None, :]
    shift_t = jnp.tile(group_shift, LAT_W)
    features = jax.nn.silu((laid - mean_t) * factor_t + shift_t).astype(jnp.bfloat16)
    return (denoised, features)


def solution(mesh):
    placed = (
        P(("sec", "rep"), None, "seq", None),
        P(("sec", "rep"), None, "seq", None),
        P(("sec", "rep"), None, "seq", None),
        P(("sec", "rep"), None),
        P(("sec", "rep"), None),
        P(),
        P(),
        P(("sec", "rep"), None, "seq", None),
        P(("sec", "rep")),
        P(),
        P(),
        P(),
        P(),
        P(),
    )
    return jax.shard_map(
        shards,
        mesh=mesh,
        in_specs=placed,
        out_specs=(P(("sec", "rep"), None, "seq", None), P(("sec", "rep"), None, "seq", None)),
        check_vma=False,
    )
```
